512 devices in a mesh: tm: 16 (over z), row: 4 (over x), col: 8 (over y, core).
Axes of the slice: x: 4, y: 4, z: 16, core: 2. Of those that a mesh axis runs over, the one named last changes fastest.
Arguments:
- latents: bfloat16 [32, 32, 256, 192], P('tm', 'row', 'col'), may hold values from -6 to 6
- first_gain: float32 [192], replicated, may hold values from 0.1 to 1.9
- first_weight: bfloat16 [3, 3, 3, 192, 192], replicated, may hold values from -0.078125 to 0.078125
- first_bias: float32 [192], replicated, may hold values from -3 to 3
- second_gain: float32 [192], replicated, may hold values from 0.1 to 1.9
- second_weight: bfloat16 [3, 3, 3, 192, 192], replicated, may hold values from -0.078125 to 0.078125
- second_bias: float32 [192], replicated, may hold values from -3 to 3
Outputs:
- decoded: bfloat16 [32, 32, 256, 192], P('tm', 'row', 'col')
The draws below stay inside these ranges and needn't reach their ends.
All inputs are finite; a program needn't handle non-finite values.
Results may differ from the reference program's by a relative error of at most 0.011.
Values may be sent and summed in bfloat16 or wider, within the bound.
No kernel may reach another device: no remote copies, remote signals or barrier semaphores. Data moves between devices by JAX's collectives and lax.ppermute only.
A program may use at most 64 MiB of HBM per device.

```python
import jax
import jax.numpy as jnp
from jax import lax

C = 192
FRAMES = 32
H = 32
W = 256


def levels(rng, dims, cuts, low, top_value):
    def one(position, blocks):
        draws = jax.random.uniform(jax.random.fold_in(jax.random.fold_in(rng, 6), position), (blocks,), jnp.float32, low / len(cuts), top_value / len(cuts))
        return jnp.repeat(jnp.exp(draws), dims[position] // blocks).reshape((-1,) + (1,) * (len(dims) - position - 1))

    level = one(*cuts[0])
    for cut in cuts[1:]:
        level = level * one(*cut)
    return level


def gaussian(key, dims, spread, limit, split=(), kind=jnp.bfloat16):
    loudness = levels(key, dims, split, -0.22, 0.18) if split else 1.0
    array = jax.random.normal(key, dims, jnp.float32) * spread * loudness
    return jnp.minimum(jnp.maximum(array, -limit), limit).astype(kind)


def setup_inputs(seed: int = 0) -> dict:
    seeds = jax.random.split(jax.random.key(seed), 8)
    latents = gaussian(seeds[0], (FRAMES, H, W, C), 1.0, 6.0, ((0, 16), (1, 4), (2, 8)))
    first_gain = jnp.clip(1.0 + 0.18 * jax.random.normal(seeds[1], (C,), jnp.float32), 0.1, 1.9)
    first_weight = gaussian(seeds[2], (3, 3, 3, C, C), (27 * C) ** -0.5, 0.078125)
    first_bias = gaussian(seeds[3], (C,), 0.5, 3.0, (), jnp.float32)
    second_gain = jnp.clip(1.0 + 0.18 * jax.random.normal(seeds[4], (C,), jnp.float32), 0.1, 1.9)
    second_weight = gaussian(seeds[5], (3, 3, 3, C, C), (27 * C) ** -0.5, 0.078125)
    second_bias = gaussian(seeds[6], (C,), 0.5, 3.0, (), jnp.float32)
    return dict(latents=latents, first_gain=first_gain, first_weight=first_weight, first_bias=first_bias, second_gain=second_gain, second_weight=second_weight, second_bias=second_bias)


def rms_norm(values, gain):
    return values * lax.rsqrt(lax.optimization_barrier(jnp.mean(values * values, axis=-1, keepdims=True)) + 1e-06) * gain

def causal_conv(activated, kernel):
    frames_all, rows, cols, chans = activated.shape
    padded = jnp.pad(activated, ((2, 0), (1, 1), (1, 1), (0, 0)))
    zero_index = jnp.zeros((), jnp.int32)

    def one_frame(index):
        accum = jnp.zeros((rows * cols, kernel.shape[-1]), jnp.float32)
        for before in range(3):
            for upward in range(3):
                for across in range(3):
                    window = lax.dynamic_slice(padded, ((index + before).astype(jnp.int32), zero_index + upward, zero_index + across, zero_index), (1, rows, cols, chans))
                    accum = accum + jnp.dot(window.reshape(rows * cols, chans), kernel[before, upward, across], preferred_element_type=jnp.float32)
        return accum
    conv = lax.map(one_frame, jnp.arange(frames_all, dtype=jnp.int32))
    return conv.reshape(frames_all, rows, cols, kernel.shape[-1])

def reference(latents, first_gain, first_weight, first_bias, second_gain, second_weight, second_bias):
    values = latents.astype(jnp.float32)
    first_act = jax.nn.silu(rms_norm(values, first_gain)).astype(jnp.bfloat16)
    hidden = (causal_conv(first_act, first_weight) + first_bias).astype(jnp.bfloat16)
    second_act = jax.nn.silu(rms_norm(hidden.astype(jnp.float32), second_gain)).astype(jnp.bfloat16)
    decoded = values + causal_conv(second_act, second_weight) + second_bias
    return decoded.astype(jnp.bfloat16)
```

```python
import jax
import jax.numpy as jnp
from jax import lax
from jax.sharding import PartitionSpec as P


def with_halo(cells, sides, width):
    for axis, dim in sides:
        count = lax.axis_size(axis)
        ends = count - 1
        head = lax.slice_in_dim(cells, 0, width, axis=dim)
        tail = lax.slice_in_dim(cells, cells.shape[dim] - width, cells.shape[dim], axis=dim)
        cells = jnp.concatenate(
            [
                lax.ppermute(tail, axis, [(i, i + 1) for i in range(ends)]),
                cells,
                lax.ppermute(head, axis, [(i + 1, i) for i in range(ends)]),
            ],
            axis=dim,
        )
    return cells


def shifted(value, axis, steps):
    count = lax.axis_size(axis)
    initial, last = (max(0, -steps), min(count, count - steps))
    return lax.ppermute(value, axis, [(source, source + steps) for source in range(initial, last)])


def rms_norm(values, gain):
    return values * lax.rsqrt(jnp.mean(values * values, axis=-1, keepdims=True) + 1e-06) * gain


def conv_valid(stack, kernel):
    out = lax.conv_general_dilated(
        stack[None],
        kernel,
        window_strides=(1, 1, 1),
        padding="VALID",
        dimension_numbers=("NDHWC", "DHWIO", "NDHWC"),
        preferred_element_type=jnp.float32,
    )
    return out[0]


def inside(axis, size, width):
    total = size * lax.axis_size(axis)
    start = lax.axis_index(axis) * size - width
    index = start + jnp.arange(size + 2 * width)
    return (index >= 0) & (index < total)


def local(latents, first_gain, first_weight, first_bias, second_gain, second_weight, second_bias):
    frames, rows, cols, chans = latents.shape
    values = latents.astype(jnp.float32)
    first_act = jax.nn.silu(rms_norm(values, first_gain)).astype(jnp.bfloat16)
    first_ext = with_halo(first_act, (("row", 1), ("col", 2)), 2)
    first_cache = shifted(first_ext, "tm", 1)
    first_conv = conv_valid(jnp.concatenate([first_cache, first_ext], axis=0), first_weight)
    hidden = (first_conv + first_bias).astype(jnp.bfloat16)
    second_act = jax.nn.silu(rms_norm(hidden.astype(jnp.float32), second_gain))
    keep = inside("row", rows, 1)[:, None] & inside("col", cols, 1)[None, :]
    second_act = jnp.where(keep[None, :, :, None], second_act, 0.0).astype(jnp.bfloat16)
    second_cache = shifted(second_act, "tm", 1)
    second_conv = conv_valid(jnp.concatenate([second_cache, second_act], axis=0), second_weight)
    decoded = values + second_conv + second_bias
    return decoded.astype(jnp.bfloat16)


def solution(mesh):
    in_specs = (P("tm", "row", "col", None), P(), P(), P(), P(), P(), P())
    out_specs = P("tm", "row", "col", None)
    return jax.shard_map(local, mesh=mesh, in_specs=in_specs, out_specs=out_specs, check_vma=False)
```

```python
import jax
import jax.numpy as jnp
from jax import lax
from jax.sharding import PartitionSpec as P


def with_halo(cells, sides, width):
    for axis, dim in sides:
        count = lax.axis_size(axis)
        ends = count - 1
        head = lax.slice_in_dim(cells, 0, width, axis=dim)
        tail = lax.slice_in_dim(cells, cells.shape[dim] - width, cells.shape[dim], axis=dim)
        cells = jnp.concatenate(
            [
                lax.ppermute(tail, axis, [(i, i + 1) for i in range(ends)]),
                cells,
                lax.ppermute(head, axis, [(i + 1, i) for i in range(ends)]),
            ],
            axis=dim,
        )
    return cells


def shifted(value, axis, steps):
    count = lax.axis_size(axis)
    initial, last = (max(0, -steps), min(count, count - steps))
    return lax.ppermute(value, axis, [(source, source + steps) for source in range(initial, last)])


def rms_norm(values, gain):
    return values * lax.rsqrt(jnp.mean(values * values, axis=-1, keepdims=True) + 1e-06) * gain


def conv_valid(stack, kernel):
    out = lax.conv_general_dilated(
        stack[None],
        kernel,
        window_strides=(1, 1, 1),
        padding="VALID",
        dimension_numbers=("NDHWC", "DHWIO", "NDHWC"),
        preferred_element_type=jnp.float32,
    )
    return out[0]


def inside(axis, size, width):
    total = size * lax.axis_size(axis)
    start = lax.axis_index(axis) * size - width
    index = start + jnp.arange(size + 2 * width)
    return (index >= 0) & (index < total)


def local(latents, first_gain, first_weight, first_bias, second_gain, second_weight, second_bias):
    frames, rows, cols, chans = latents.shape
    values = latents.astype(jnp.float32)
    first_act = jax.nn.silu(rms_norm(values, first_gain)).astype(jnp.bfloat16)
    stack = jnp.concatenate(
        [shifted(first_act, "tm", 2), shifted(first_act, "tm", 1), first_act], axis=0
    )
    first_ext = with_halo(stack, (("row", 1), ("col", 2)), 2)
    first_conv = conv_valid(first_ext, first_weight)
    hidden = (first_conv + first_bias).astype(jnp.bfloat16)
    second_act = jax.nn.silu(rms_norm(hidden.astype(jnp.float32), second_gain))
    early = lax.axis_index("tm") * frames - 2 + jnp.arange(2 * frames) >= 0
    keep = inside("row", rows, 1)[:, None] & inside("col", cols, 1)[None, :]
    keep = early[:, None, None] & keep[None]
    second_act = jnp.where(keep[..., None], second_act, 0.0).astype(jnp.bfloat16)
    second_conv = conv_valid(second_act, second_weight)
    decoded = values + second_conv + second_bias
    return decoded.astype(jnp.bfloat16)


def solution(mesh):
    in_specs = (P("tm", "row", "col", None), P(), P(), P(), P(), P(), P())
    out_specs = P("tm", "row", "col", None)
    return jax.shard_map(local, mesh=mesh, in_specs=in_specs, out_specs=out_specs, check_vma=False)
```

```python
import jax
import jax.numpy as jnp
from jax import lax
from jax.sharding import PartitionSpec as P


def with_halo(cells, sides, width):
    for axis, dim in sides:
        count = lax.axis_size(axis)
        ends = count - 1
        head = lax.slice_in_dim(cells, 0, width, axis=dim)
        tail = lax.slice_in_dim(cells, cells.shape[dim] - width, cells.shape[dim], axis=dim)
        cells = jnp.concatenate(
            [
                lax.ppermute(tail, axis, [(i, i + 1) for i in range(ends)]),
                cells,
                lax.ppermute(head, axis, [(i + 1, i) for i in range(ends)]),
            ],
            axis=dim,
        )
    return cells


def shifted(value, axis, steps):
    count = lax.axis_size(axis)
    initial, last = (max(0, -steps), min(count, count - steps))
    return lax.ppermute(value, axis, [(source, source + steps) for source in range(initial, last)])


def rms_norm(values, gain):
    return values * lax.rsqrt(jnp.mean(values * values, axis=-1, keepdims=True) + 1e-06) * gain


def conv_valid(stack, kernel):
    out = lax.conv_general_dilated(
        stack[None],
        kernel,
        window_strides=(1, 1, 1),
        padding="VALID",
        dimension_numbers=("NDHWC", "DHWIO", "NDHWC"),
        preferred_element_type=jnp.float32,
    )
    return out[0]


def inside(axis, size, width):
    total = size * lax.axis_size(axis)
    start = lax.axis_index(axis) * size - width
    index = start + jnp.arange(size + 2 * width)
    return (index >= 0) & (index < total)


def local(latents, first_gain, first_weight, first_bias, second_gain, second_weight, second_bias):
    frames, rows, cols, chans = latents.shape
    values = latents.astype(jnp.float32)
    first_act = jax.nn.silu(rms_norm(values, first_gain)).astype(jnp.bfloat16)
    stack = jnp.concatenate([shifted(first_act, "tm", 1), first_act], axis=0)
    first_ext = with_halo(stack, (("row", 1), ("col", 2)), 2)
    first_conv = conv_valid(first_ext, first_weight)
    hidden = (first_conv + first_bias).astype(jnp.bfloat16)
    second_act = jax.nn.silu(rms_norm(hidden.astype(jnp.float32), second_gain))
    keep = inside("row", rows, 1)[:, None] & inside("col", cols, 1)[None, :]
    second_act = jnp.where(keep[None, :, :, None], second_act, 0.0).astype(jnp.bfloat16)
    second_cache = shifted(second_act, "tm", 1)
    second_conv = conv_valid(jnp.concatenate([second_cache, second_act], axis=0), second_weight)
    decoded = values + second_conv + second_bias
    return decoded.astype(jnp.bfloat16)


def solution(mesh):
    in_specs = (P("tm", "row", "col", None), P(), P(), P(), P(), P(), P())
    out_specs = P("tm", "row", "col", None)
    return jax.shard_map(local, mesh=mesh, in_specs=in_specs, out_specs=out_specs, check_vma=False)
```

```python
import jax
import jax.numpy as jnp
from jax import lax
from jax.experimental import pallas as pl
from jax.sharding import PartitionSpec as P


def with_halo(cells, sides, width):
    for axis, dim in sides:
        count = lax.axis_size(axis)
        ends = count - 1
        head = lax.slice_in_dim(cells, 0, width, axis=dim)
        tail = lax.slice_in_dim(cells, cells.shape[dim] - width, cells.shape[dim], axis=dim)
        cells = jnp.concatenate(
            [
                lax.ppermute(tail, axis, [(i, i + 1) for i in range(ends)]),
                cells,
                lax.ppermute(head, axis, [(i + 1, i) for i in range(ends)]),
            ],
            axis=dim,
        )
    return cells


def shifted(value, axis, steps):
    count = lax.axis_size(axis)
    initial, last = (max(0, -steps), min(count, count - steps))
    return lax.ppermute(value, axis, [(source, source + steps) for source in range(initial, last)])


def rms_norm(values, gain):
    return values * lax.rsqrt(jnp.mean(values * values, axis=-1, keepdims=True) + 1e-06) * gain


def _act_kernel(x_ref, gain_ref, bias_ref, keep_ref, out_ref, *, rounded):
    values = x_ref[...].astype(jnp.float32) + bias_ref[...]
    if rounded:
        values = values.astype(jnp.bfloat16).astype(jnp.float32)
    scale = lax.rsqrt(jnp.mean(values * values, axis=-1, keepdims=True) + 1e-06)
    normed = values * scale * gain_ref[...]
    act = normed / (1.0 + jnp.exp(-normed))
    out_ref[...] = (act * keep_ref[...]).astype(out_ref.dtype)


def activation(cells, gain, bias, keep, rounded):
    shape = cells.shape
    flat = cells.reshape(-1, shape[-1])
    out = pl.pallas_call(
        lambda *refs: _act_kernel(*refs, rounded=rounded),
        out_shape=jax.ShapeDtypeStruct(flat.shape, jnp.bfloat16),
    )(flat, gain.reshape(1, -1), bias.reshape(1, -1), keep.reshape(-1, 1).astype(jnp.float32))
    return out.reshape(shape)


def _residual_kernel(x_ref, conv_ref, bias_ref, out_ref):
    out_ref[...] = (x_ref[...].astype(jnp.float32) + conv_ref[...] + bias_ref[...]).astype(out_ref.dtype)


def residual(latents, conv, bias):
    shape = latents.shape
    out = pl.pallas_call(
        _residual_kernel,
        out_shape=jax.ShapeDtypeStruct((shape[0] * shape[1] * shape[2], shape[3]), latents.dtype),
    )(latents.reshape(-1, shape[-1]), conv.reshape(-1, shape[-1]), bias.reshape(1, -1))
    return out.reshape(shape)


def conv_valid(stack, kernel):
    out = lax.conv_general_dilated(
        stack[None],
        kernel,
        window_strides=(1, 1, 1),
        padding="VALID",
        dimension_numbers=("NDHWC", "DHWIO", "NDHWC"),
        preferred_element_type=jnp.float32,
    )
    return out[0]


def inside(axis, size, width):
    total = size * lax.axis_size(axis)
    start = lax.axis_index(axis) * size - width
    index = start + jnp.arange(size + 2 * width)
    return (index >= 0) & (index < total)


def local(latents, first_gain, first_weight, first_bias, second_gain, second_weight, second_bias):
    frames, rows, cols, chans = latents.shape
    ones = jnp.ones((frames, rows, cols), jnp.float32)
    first_act = activation(latents, first_gain, jnp.zeros_like(first_bias), ones, False)
    stack = jnp.concatenate([shifted(first_act, "tm", 1), first_act], axis=0)
    first_ext = with_halo(stack, (("row", 1), ("col", 2)), 2)
    first_conv = conv_valid(first_ext, first_weight)
    keep = inside("row", rows, 1)[:, None] & inside("col", cols, 1)[None, :]
    keep = jnp.broadcast_to(keep[None], first_conv.shape[:3])
    second_act = activation(first_conv, second_gain, first_bias, keep, True)
    second_cache = shifted(second_act, "tm", 1)
    second_conv = conv_valid(jnp.concatenate([second_cache, second_act], axis=0), second_weight)
    return residual(latents, second_conv, second_bias)


def solution(mesh):
    in_specs = (P("tm", "row", "col", None), P(), P(), P(), P(), P(), P())
    out_specs = P("tm", "row", "col", None)
    return jax.shard_map(local, mesh=mesh, in_specs=in_specs, out_specs=out_specs, check_vma=False)
```

```python
import jax
import jax.numpy as jnp
from jax import lax
from jax.sharding import PartitionSpec as P


def with_halo(cells, sides, width):
    for axis, dim in sides:
        count = lax.axis_size(axis)
        ends = count - 1
        head = lax.slice_in_dim(cells, 0, width, axis=dim)
        tail = lax.slice_in_dim(cells, cells.shape[dim] - width, cells.shape[dim], axis=dim)
        cells = jnp.concatenate(
            [
                lax.ppermute(tail, axis, [(i, i + 1) for i in range(ends)]),
                cells,
                lax.ppermute(head, axis, [(i + 1, i) for i in range(ends)]),
            ],
            axis=dim,
        )
    return cells


def shifted(value, axis, steps):
    count = lax.axis_size(axis)
    initial, last = (max(0, -steps), min(count, count - steps))
    return lax.ppermute(value, axis, [(source, source + steps) for source in range(initial, last)])


def own_wide(cells, width):
    count = lax.axis_size("col")
    head = cells[:, :, :width]
    tail = cells[:, :, cells.shape[2] - width :]
    from_left = lax.ppermute(tail, "col", [(i, i + 1) for i in range(count - 1)])
    from_right = lax.ppermute(head, "col", [(i + 1, i) for i in range(count - 1)])
    return jnp.concatenate([from_left, cells, from_right], axis=2)


def previous_wide(cells, width):
    groups = lax.axis_size("tm")
    count = lax.axis_size("col")
    head = cells[:, :, :width]
    tail = cells[:, :, cells.shape[2] - width :]

    def place(group, column):
        return group * count + column

    middle = lax.ppermute(cells, "tm", [(g, g + 1) for g in range(groups - 1)])
    from_left = lax.ppermute(
        tail,
        ("tm", "col"),
        [(place(g, c), place(g + 1, c + 1)) for g in range(groups - 1) for c in range(count - 1)],
    )
    from_right = lax.ppermute(
        head,
        ("tm", "col"),
        [(place(g, c + 1), place(g + 1, c)) for g in range(groups - 1) for c in range(count - 1)],
    )
    return jnp.concatenate([from_left, middle, from_right], axis=2)


def rms_norm(values, gain):
    return values * lax.rsqrt(jnp.mean(values * values, axis=-1, keepdims=True) + 1e-06) * gain


def conv_valid(stack, kernel):
    out = lax.conv_general_dilated(
        stack[None],
        kernel,
        window_strides=(1, 1, 1),
        padding="VALID",
        dimension_numbers=("NDHWC", "DHWIO", "NDHWC"),
        preferred_element_type=jnp.float32,
    )
    return out[0]


def inside(axis, size, width):
    total = size * lax.axis_size(axis)
    start = lax.axis_index(axis) * size - width
    index = start + jnp.arange(size + 2 * width)
    return (index >= 0) & (index < total)


def local(latents, first_gain, first_weight, first_bias, second_gain, second_weight, second_bias):
    frames, rows, cols, chans = latents.shape
    values = latents.astype(jnp.float32)
    first_act = jax.nn.silu(rms_norm(values, first_gain)).astype(jnp.bfloat16)
    stack = jnp.concatenate([previous_wide(first_act, 2), own_wide(first_act, 2)], axis=0)
    first_ext = with_halo(stack, (("row", 1),), 2)
    first_conv = conv_valid(first_ext, first_weight)
    hidden = (first_conv + first_bias).astype(jnp.bfloat16)
    second_act = jax.nn.silu(rms_norm(hidden.astype(jnp.float32), second_gain))
    keep = inside("row", rows, 1)[:, None] & inside("col", cols, 1)[None, :]
    second_act = jnp.where(keep[None, :, :, None], second_act, 0.0).astype(jnp.bfloat16)
    second_cache = shifted(second_act, "tm", 1)
    second_conv = conv_valid(jnp.concatenate([second_cache, second_act], axis=0), second_weight)
    decoded = values + second_conv + second_bias
    return decoded.astype(jnp.bfloat16)


def solution(mesh):
    in_specs = (P("tm", "row", "col", None), P(), P(), P(), P(), P(), P())
    out_specs = P("tm", "row", "col", None)
    return jax.shard_map(local, mesh=mesh, in_specs=in_specs, out_specs=out_specs, check_vma=False)
```

```python
import jax
import jax.numpy as jnp
from jax import lax
from jax.sharding import PartitionSpec as P


def with_halo(cells, sides, width):
    for axis, dim in sides:
        count = lax.axis_size(axis)
        ends = count - 1
        head = lax.slice_in_dim(cells, 0, width, axis=dim)
        tail = lax.slice_in_dim(cells, cells.shape[dim] - width, cells.shape[dim], axis=dim)
        cells = jnp.concatenate(
            [
                lax.ppermute(tail, axis, [(i, i + 1) for i in range(ends)]),
                cells,
                lax.ppermute(head, axis, [(i + 1, i) for i in range(ends)]),
            ],
            axis=dim,
        )
    return cells


def rows_exchanged(cells, width):
    count = lax.axis_size("row")
    here = lax.axis_index("row")
    head = lax.slice_in_dim(cells, 0, width, axis=1)
    tail = lax.slice_in_dim(cells, cells.shape[1] - width, cells.shape[1], axis=1)
    target = jnp.arange(count)[:, None, None, None, None]
    chunks = jnp.where(target == here - 1, head[None], jnp.where(target == here + 1, tail[None], 0))
    got = lax.all_to_all(chunks.astype(cells.dtype), "row", 0, 0)
    above = jnp.where(here > 0, lax.dynamic_index_in_dim(got, jnp.maximum(here - 1, 0), 0, False), 0)
    below = jnp.where(
        here < count - 1, lax.dynamic_index_in_dim(got, jnp.minimum(here + 1, count - 1), 0, False), 0
    )
    return jnp.concatenate([above.astype(cells.dtype), cells, below.astype(cells.dtype)], axis=1)


def shifted(value, axis, steps):
    count = lax.axis_size(axis)
    initial, last = (max(0, -steps), min(count, count - steps))
    return lax.ppermute(value, axis, [(source, source + steps) for source in range(initial, last)])


def rms_norm(values, gain):
    return values * lax.rsqrt(jnp.mean(values * values, axis=-1, keepdims=True) + 1e-06) * gain


def conv_valid(stack, kernel):
    out = lax.conv_general_dilated(
        stack[None],
        kernel,
        window_strides=(1, 1, 1),
        padding="VALID",
        dimension_numbers=("NDHWC", "DHWIO", "NDHWC"),
        preferred_element_type=jnp.float32,
    )
    return out[0]


def inside(axis, size, width):
    total = size * lax.axis_size(axis)
    start = lax.axis_index(axis) * size - width
    index = start + jnp.arange(size + 2 * width)
    return (index >= 0) & (index < total)


def local(latents, first_gain, first_weight, first_bias, second_gain, second_weight, second_bias):
    frames, rows, cols, chans = latents.shape
    values = latents.astype(jnp.float32)
    first_act = jax.nn.silu(rms_norm(values, first_gain)).astype(jnp.bfloat16)
    stack = jnp.concatenate([shifted(first_act, "tm", 1), first_act], axis=0)
    first_ext = with_halo(rows_exchanged(stack, 2), (("col", 2),), 2)
    first_conv = conv_valid(first_ext, first_weight)
    hidden = (first_conv + first_bias).astype(jnp.bfloat16)
    second_act = jax.nn.silu(rms_norm(hidden.astype(jnp.float32), second_gain))
    keep = inside("row", rows, 1)[:, None] & inside("col", cols, 1)[None, :]
    second_act = jnp.where(keep[None, :, :, None], second_act, 0.0).astype(jnp.bfloat16)
    second_cache = shifted(second_act, "tm", 1)
    second_conv = conv_valid(jnp.concatenate([second_cache, second_act], axis=0), second_weight)
    decoded = values + second_conv + second_bias
    return decoded.astype(jnp.bfloat16)


def solution(mesh):
    in_specs = (P("tm", "row", "col", None), P(), P(), P(), P(), P(), P())
    out_specs = P("tm", "row", "col", None)
    return jax.shard_map(local, mesh=mesh, in_specs=in_specs, out_specs=out_specs, check_vma=False)
```

```python
import jax
import jax.numpy as jnp
from jax import lax
from jax.sharding import PartitionSpec as P


def with_halo(cells, sides, width):
    for axis, dim in sides:
        count = lax.axis_size(axis)
        ends = count - 1
        head = lax.slice_in_dim(cells, 0, width, axis=dim)
        tail = lax.slice_in_dim(cells, cells.shape[dim] - width, cells.shape[dim], axis=dim)
        cells = jnp.concatenate(
            [
                lax.ppermute(tail, axis, [(i, i + 1) for i in range(ends)]),
                cells,
                lax.ppermute(head, axis, [(i + 1, i) for i in range(ends)]),
            ],
            axis=dim,
        )
    return cells


def shifted(value, axis, steps):
    count = lax.axis_size(axis)
    initial, last = (max(0, -steps), min(count, count - steps))
    return lax.ppermute(value, axis, [(source, source + steps) for source in range(initial, last)])


def rms_norm(values, gain):
    chans = values.shape[-1]
    total = jnp.dot(values * values, jnp.ones((chans, 1), jnp.float32), precision=lax.Precision.HIGHEST)
    return values * lax.rsqrt(total / chans + 1e-06) * gain


def silu(values):
    return values * (0.5 * jnp.tanh(0.5 * values) + 0.5)


def conv_valid(stack, kernel):
    out = lax.conv_general_dilated(
        stack[None],
        kernel,
        window_strides=(1, 1, 1),
        padding="VALID",
        dimension_numbers=("NDHWC", "DHWIO", "NDHWC"),
        preferred_element_type=jnp.float32,
    )
    return out[0]


def inside(axis, size, width):
    total = size * lax.axis_size(axis)
    start = lax.axis_index(axis) * size - width
    index = start + jnp.arange(size + 2 * width)
    return (index >= 0) & (index < total)


def local(latents, first_gain, first_weight, first_bias, second_gain, second_weight, second_bias):
    frames, rows, cols, chans = latents.shape
    values = latents.astype(jnp.float32)
    first_act = silu(rms_norm(values, first_gain)).astype(jnp.bfloat16)
    stack = jnp.concatenate([shifted(first_act, "tm", 1), first_act], axis=0)
    first_ext = with_halo(stack, (("row", 1), ("col", 2)), 2)
    first_conv = conv_valid(first_ext, first_weight)
    hidden = (first_conv + first_bias).astype(jnp.bfloat16)
    second_act = silu(rms_norm(hidden.astype(jnp.float32), second_gain))
    keep = inside("row", rows, 1)[:, None] & inside("col", cols, 1)[None, :]
    second_act = jnp.where(keep[None, :, :, None], second_act, 0.0).astype(jnp.bfloat16)
    second_cache = shifted(second_act, "tm", 1)
    second_conv = conv_valid(jnp.concatenate([second_cache, second_act], axis=0), second_weight)
    decoded = values + second_conv + second_bias
    return decoded.astype(jnp.bfloat16)


def solution(mesh):
    in_specs = (P("tm", "row", "col", None), P(), P(), P(), P(), P(), P())
    out_specs = P("tm", "row", "col", None)
    return jax.shard_map(local, mesh=mesh, in_specs=in_specs, out_specs=out_specs, check_vma=False)
```

```python
import jax
import jax.numpy as jnp
from jax import lax
from jax.sharding import PartitionSpec as P


def with_halo(cells, sides, width):
    for axis, dim in sides:
        count = lax.axis_size(axis)
        ends = count - 1
        head = lax.slice_in_dim(cells, 0, width, axis=dim)
        tail = lax.slice_in_dim(cells, cells.shape[dim] - width, cells.shape[dim], axis=dim)
        cells = jnp.concatenate(
            [
                lax.ppermute(tail, axis, [(i, i + 1) for i in range(ends)]),
                cells,
                lax.ppermute(head, axis, [(i + 1, i) for i in range(ends)]),
            ],
            axis=dim,
        )
    return cells


def shifted(value, axis, steps):
    count = lax.axis_size(axis)
    initial, last = (max(0, -steps), min(count, count - steps))
    return lax.ppermute(value, axis, [(source, source + steps) for source in range(initial, last)])


def rms_norm(values, gain):
    return values * lax.rsqrt(jnp.mean(values * values, axis=-1, keepdims=True) + 1e-06) * gain


def conv_valid(stack, kernel, frame_pad=(0, 0)):
    out = lax.conv_general_dilated(
        stack[None],
        kernel,
        window_strides=(1, 1, 1),
        padding=(frame_pad, (0, 0), (0, 0)),
        dimension_numbers=("NDHWC", "DHWIO", "NDHWC"),
        preferred_element_type=jnp.float32,
    )
    return out[0]


def inside(axis, size, width):
    total = size * lax.axis_size(axis)
    start = lax.axis_index(axis) * size - width
    index = start + jnp.arange(size + 2 * width)
    return (index >= 0) & (index < total)


def local(latents, first_gain, first_weight, first_bias, second_gain, second_weight, second_bias):
    frames, rows, cols, chans = latents.shape
    values = latents.astype(jnp.float32)
    first_act = jax.nn.silu(rms_norm(values, first_gain)).astype(jnp.bfloat16)
    stack = jnp.concatenate([shifted(first_act, "tm", 1), first_act], axis=0)
    first_ext = with_halo(stack, (("row", 1), ("col", 2)), 2)
    first_conv = conv_valid(first_ext, first_weight)
    hidden = (first_conv + first_bias).astype(jnp.bfloat16)
    second_act = jax.nn.silu(rms_norm(hidden.astype(jnp.float32), second_gain))
    keep = inside("row", rows, 1)[:, None] & inside("col", cols, 1)[None, :]
    second_act = jnp.where(keep[None, :, :, None], second_act, 0.0).astype(jnp.bfloat16)
    ahead = conv_valid(second_act, second_weight[0:2], (0, 1)).astype(jnp.bfloat16)
    behind = shifted(ahead, "tm", 1)
    own = conv_valid(second_act, second_weight[1:3], (1, 0))
    decoded = values + own + behind.astype(jnp.float32) + second_bias
    return decoded.astype(jnp.bfloat16)


def solution(mesh):
    in_specs = (P("tm", "row", "col", None), P(), P(), P(), P(), P(), P())
    out_specs = P("tm", "row", "col", None)
    return jax.shard_map(local, mesh=mesh, in_specs=in_specs, out_specs=out_specs, check_vma=False)
```

```python
import jax
import jax.numpy as jnp
from jax import lax
from jax.sharding import PartitionSpec as P


def with_halo(cells, sides, width):
    for axis, dim in sides:
        count = lax.axis_size(axis)
        even = lax.axis_index(axis) % 2 == 0
        head = lax.slice_in_dim(cells, 0, width, axis=dim)
        tail = lax.slice_in_dim(cells, cells.shape[dim] - width, cells.shape[dim], axis=dim)
        first = [(i, i ^ 1) for i in range(count - count % 2)]
        second = [(i, i + 1 if i % 2 else i - 1) for i in range(1, count - 1)]
        got_first = lax.ppermute(jnp.where(even, tail, head), axis, first)
        got_second = lax.ppermute(jnp.where(even, head, tail), axis, second)
        cells = jnp.concatenate(
            [
                jnp.where(even, got_second, got_first),
                cells,
                jnp.where(even, got_first, got_second),
            ],
            axis=dim,
        )
    return cells


def shifted(value, axis, steps):
    count = lax.axis_size(axis)
    initial, last = (max(0, -steps), min(count, count - steps))
    return lax.ppermute(value, axis, [(source, source + steps) for source in range(initial, last)])


def rms_norm(values, gain):
    return values * lax.rsqrt(jnp.mean(values * values, axis=-1, keepdims=True) + 1e-06) * gain


def conv_valid(stack, kernel, frame_pad=(0, 0)):
    out = lax.conv_general_dilated(
        stack[None],
        kernel,
        window_strides=(1, 1, 1),
        padding=(frame_pad, (0, 0), (0, 0)),
        dimension_numbers=("NDHWC", "DHWIO", "NDHWC"),
        preferred_element_type=jnp.float32,
    )
    return out[0]


def conv_folded(stack, kernel):
    taps = kernel.shape[0]
    count = stack.shape[0] - taps + 1
    wide = jnp.concatenate([stack[p : p + count] for p in range(taps)], axis=-1)
    folded = jnp.transpose(kernel, (1, 2, 0, 3, 4)).reshape(
        kernel.shape[1], kernel.shape[2], taps * kernel.shape[3], kernel.shape[4]
    )
    return lax.conv_general_dilated(
        wide,
        folded,
        window_strides=(1, 1),
        padding="VALID",
        dimension_numbers=("NHWC", "HWIO", "NHWC"),
        preferred_element_type=jnp.float32,
    )


def inside(axis, size, width):
    total = size * lax.axis_size(axis)
    start = lax.axis_index(axis) * size - width
    index = start + jnp.arange(size + 2 * width)
    return (index >= 0) & (index < total)


def local(latents, first_gain, first_weight, first_bias, second_gain, second_weight, second_bias):
    frames, rows, cols, chans = latents.shape
    values = latents.astype(jnp.float32)
    first_act = jax.nn.silu(rms_norm(values, first_gain)).astype(jnp.bfloat16)
    stack = jnp.concatenate([shifted(first_act, "tm", 1), first_act], axis=0)
    first_ext = with_halo(stack, (("row", 1), ("col", 2)), 2)
    first_conv = conv_folded(first_ext, first_weight)
    hidden = (first_conv + first_bias).astype(jnp.bfloat16)
    second_act = jax.nn.silu(rms_norm(hidden.astype(jnp.float32), second_gain))
    keep = inside("row", rows, 1)[:, None] & inside("col", cols, 1)[None, :]
    second_act = jnp.where(keep[None, :, :, None], second_act, 0.0).astype(jnp.bfloat16)
    ahead = conv_valid(second_act, second_weight[0:2], (0, 1)).astype(jnp.bfloat16)
    behind = shifted(ahead, "tm", 1)
    own = conv_valid(second_act, second_weight[1:3], (1, 0))
    decoded = values + own + behind.astype(jnp.float32) + second_bias
    return decoded.astype(jnp.bfloat16)


def solution(mesh):
    in_specs = (P("tm", "row", "col", None), P(), P(), P(), P(), P(), P())
    out_specs = P("tm", "row", "col", None)
    return jax.shard_map(local, mesh=mesh, in_specs=in_specs, out_specs=out_specs, check_vma=False)
```

```python
import jax
import jax.numpy as jnp
from jax import lax
from jax.sharding import PartitionSpec as P


def with_halo(cells, sides, width):
    for axis, dim in sides:
        count = lax.axis_size(axis)
        here = lax.axis_index(axis)
        head = lax.slice_in_dim(cells, 0, width, axis=dim)
        tail = lax.slice_in_dim(cells, cells.shape[dim] - width, cells.shape[dim], axis=dim)
        before = lax.ppermute(tail, axis, [(i, (i + 1) % count) for i in range(count)])
        after = lax.ppermute(head, axis, [((i + 1) % count, i) for i in range(count)])
        cells = jnp.concatenate(
            [
                jnp.where(here > 0, before, jnp.zeros_like(before)),
                cells,
                jnp.where(here < count - 1, after, jnp.zeros_like(after)),
            ],
            axis=dim,
        )
    return cells


def shifted(value, axis, steps):
    count = lax.axis_size(axis)
    moved = lax.ppermute(value, axis, [(i, (i + 1) % count) for i in range(count)])
    return jnp.where(lax.axis_index(axis) > 0, moved, jnp.zeros_like(moved))


def rms_norm(values, gain):
    return values * lax.rsqrt(jnp.mean(values * values, axis=-1, keepdims=True) + 1e-06) * gain


def conv_valid(stack, kernel, frame_pad=(0, 0)):
    out = lax.conv_general_dilated(
        stack[None],
        kernel,
        window_strides=(1, 1, 1),
        padding=(frame_pad, (0, 0), (0, 0)),
        dimension_numbers=("NDHWC", "DHWIO", "NDHWC"),
        preferred_element_type=jnp.float32,
    )
    return out[0]


def inside(axis, size, width):
    total = size * lax.axis_size(axis)
    start = lax.axis_index(axis) * size - width
    index = start + jnp.arange(size + 2 * width)
    return (index >= 0) & (index < total)


def local(latents, first_gain, first_weight, first_bias, second_gain, second_weight, second_bias):
    frames, rows, cols, chans = latents.shape
    values = latents.astype(jnp.float32)
    first_act = jax.nn.silu(rms_norm(values, first_gain)).astype(jnp.bfloat16)
    stack = jnp.concatenate([shifted(first_act, "tm", 1), first_act], axis=0)
    first_ext = with_halo(stack, (("row", 1), ("col", 2)), 2)
    first_conv = conv_valid(first_ext, first_weight)
    hidden = (first_conv + first_bias).astype(jnp.bfloat16)
    second_act = jax.nn.silu(rms_norm(hidden.astype(jnp.float32), second_gain))
    keep = inside("row", rows, 1)[:, None] & inside("col", cols, 1)[None, :]
    second_act = jnp.where(keep[None, :, :, None], second_act, 0.0).astype(jnp.bfloat16)
    ahead = conv_valid(second_act, second_weight[0:2], (0, 1)).astype(jnp.bfloat16)
    behind = shifted(ahead, "tm", 1)
    own = conv_valid(second_act, second_weight[1:3], (1, 0))
    decoded = values + own + behind.astype(jnp.float32) + second_bias
    return decoded.astype(jnp.bfloat16)


def solution(mesh):
    in_specs = (P("tm", "row", "col", None), P(), P(), P(), P(), P(), P())
    out_specs = P("tm", "row", "col", None)
    return jax.shard_map(local, mesh=mesh, in_specs=in_specs, out_specs=out_specs, check_vma=False)
```

```python
import jax
import jax.numpy as jnp
from jax import lax
from jax.sharding import PartitionSpec as P


def with_halo(cells, sides, width):
    for axis, dim in sides:
        count = lax.axis_size(axis)
        ends = count - 1
        head = lax.slice_in_dim(cells, 0, width, axis=dim)
        tail = lax.slice_in_dim(cells, cells.shape[dim] - width, cells.shape[dim], axis=dim)
        cells = jnp.concatenate(
            [
                lax.ppermute(tail, axis, [(i, i + 1) for i in range(ends)]),
                cells,
                lax.ppermute(head, axis, [(i + 1, i) for i in range(ends)]),
            ],
            axis=dim,
        )
    return cells


def shifted(value, axis, steps):
    count = lax.axis_size(axis)
    initial, last = (max(0, -steps), min(count, count - steps))
    return lax.ppermute(value, axis, [(source, source + steps) for source in range(initial, last)])


def rms_norm(values, gain):
    return values * lax.rsqrt(jnp.mean(values * values, axis=-1, keepdims=True) + 1e-06) * gain


def conv_valid(stack, kernel, frame_pad=(0, 0)):
    out = lax.conv_general_dilated(
        stack[None],
        kernel,
        window_strides=(1, 1, 1),
        padding=(frame_pad, (0, 0), (0, 0)),
        dimension_numbers=("NDHWC", "DHWIO", "NDHWC"),
        preferred_element_type=jnp.float32,
    )
    return out[0]


def inside(axis, size, width):
    total = size * lax.axis_size(axis)
    start = lax.axis_index(axis) * size - width
    index = start + jnp.arange(size + 2 * width)
    return (index >= 0) & (index < total)


def local(latents, first_gain, first_weight, first_bias, second_gain, second_weight, second_bias):
    frames, rows, cols, chans = latents.shape
    values = latents.astype(jnp.float32)
    first_act = jax.nn.silu(rms_norm(values, first_gain)).astype(jnp.bfloat16)
    stack = jnp.concatenate([shifted(first_act, "tm", 1), first_act], axis=0)
    first_ext = with_halo(stack, (("col", 2), ("row", 1)), 2)
    first_conv = conv_valid(first_ext, first_weight)
    hidden = (first_conv + first_bias).astype(jnp.bfloat16)
    second_act = jax.nn.silu(rms_norm(hidden.astype(jnp.float32), second_gain))
    keep = inside("row", rows, 1)[:, None] & inside("col", cols, 1)[None, :]
    second_act = jnp.where(keep[None, :, :, None], second_act, 0.0).astype(jnp.bfloat16)
    ahead = conv_valid(second_act, second_weight[0:2], (0, 1)).astype(jnp.bfloat16)
    behind = shifted(ahead, "tm", 1)
    own = conv_valid(second_act, second_weight[1:3], (1, 0))
    decoded = values + own + behind.astype(jnp.float32) + second_bias
    return decoded.astype(jnp.bfloat16)


def solution(mesh):
    in_specs = (P("tm", "row", "col", None), P(), P(), P(), P(), P(), P())
    out_specs = P("tm", "row", "col", None)
    return jax.shard_map(local, mesh=mesh, in_specs=in_specs, out_specs=out_specs, check_vma=False)
```

```python
import jax
import jax.numpy as jnp
from jax import lax
from jax.sharding import PartitionSpec as P


def with_halo(cells, sides, width):
    for axis, dim in sides:
        count = lax.axis_size(axis)
        ends = count - 1
        head = lax.slice_in_dim(cells, 0, width, axis=dim)
        tail = lax.slice_in_dim(cells, cells.shape[dim] - width, cells.shape[dim], axis=dim)
        cells = jnp.concatenate(
            [
                lax.ppermute(tail, axis, [(i, i + 1) for i in range(ends)]),
                cells,
                lax.ppermute(head, axis, [(i + 1, i) for i in range(ends)]),
            ],
            axis=dim,
        )
    return cells


def shifted(value, axis, steps):
    count = lax.axis_size(axis)
    initial, last = (max(0, -steps), min(count, count - steps))
    return lax.ppermute(value, axis, [(source, source + steps) for source in range(initial, last)])


def rms_norm(values, gain):
    return values * lax.rsqrt(jnp.mean(values * values, axis=-1, keepdims=True) + 1e-06) * gain


def conv_valid(stack, kernel, frame_pad=(0, 0)):
    out = lax.conv_general_dilated(
        stack[None],
        kernel,
        window_strides=(1, 1, 1),
        padding=(frame_pad, (0, 0), (0, 0)),
        dimension_numbers=("NDHWC", "DHWIO", "NDHWC"),
        preferred_element_type=jnp.float32,
    )
    return out[0]


def inside(axis, size, width):
    total = size * lax.axis_size(axis)
    start = lax.axis_index(axis) * size - width
    index = start + jnp.arange(size + 2 * width)
    return (index >= 0) & (index < total)


def local(latents, first_gain, first_weight, first_bias, second_gain, second_weight, second_bias):
    frames, rows, cols, chans = latents.shape
    values = latents.astype(jnp.float32)
    first_act = jax.nn.silu(rms_norm(values, first_gain)).astype(jnp.bfloat16)
    stack = jnp.concatenate([shifted(first_act, "tm", 1), first_act], axis=0)
    wide = with_halo(stack, (("col", 2),), 2)
    middle = conv_valid(wide, first_weight)
    first_ext = with_halo(wide, (("row", 1),), 2)
    edge = 2 * 2
    top = conv_valid(first_ext[:, :edge], first_weight)
    bottom = conv_valid(first_ext[:, first_ext.shape[1] - edge :], first_weight)
    first_conv = jnp.concatenate([top, middle, bottom], axis=1)
    hidden = (first_conv + first_bias).astype(jnp.bfloat16)
    second_act = jax.nn.silu(rms_norm(hidden.astype(jnp.float32), second_gain))
    keep = inside("row", rows, 1)[:, None] & inside("col", cols, 1)[None, :]
    second_act = jnp.where(keep[None, :, :, None], second_act, 0.0).astype(jnp.bfloat16)
    ahead = conv_valid(second_act, second_weight[0:2], (0, 1)).astype(jnp.bfloat16)
    behind = shifted(ahead, "tm", 1)
    own = conv_valid(second_act, second_weight[1:3], (1, 0))
    decoded = values + own + behind.astype(jnp.float32) + second_bias
    return decoded.astype(jnp.bfloat16)


def solution(mesh):
    in_specs = (P("tm", "row", "col", None), P(), P(), P(), P(), P(), P())
    out_specs = P("tm", "row", "col", None)
    return jax.shard_map(local, mesh=mesh, in_specs=in_specs, out_specs=out_specs, check_vma=False)
```

```python
import jax
import jax.numpy as jnp
from jax import lax
from jax.sharding import PartitionSpec as P


def with_halo(cells, sides, width):
    for axis, dim in sides:
        count = lax.axis_size(axis)
        ends = count - 1
        head = lax.slice_in_dim(cells, 0, width, axis=dim)
        tail = lax.slice_in_dim(cells, cells.shape[dim] - width, cells.shape[dim], axis=dim)
        cells = jnp.concatenate(
            [
                lax.ppermute(tail, axis, [(i, i + 1) for i in range(ends)]),
                cells,
                lax.ppermute(head, axis, [(i + 1, i) for i in range(ends)]),
            ],
            axis=dim,
        )
    return cells


def shifted(value, axis, steps):
    count = lax.axis_size(axis)
    initial, last = (max(0, -steps), min(count, count - steps))
    return lax.ppermute(value, axis, [(source, source + steps) for source in range(initial, last)])


def rms_norm(values, gain):
    return values * lax.rsqrt(jnp.mean(values * values, axis=-1, keepdims=True) + 1e-06) * gain


def conv_valid(stack, kernel, frame_pad=(0, 0)):
    out = lax.conv_general_dilated(
        stack[None],
        kernel,
        window_strides=(1, 1, 1),
        padding=(frame_pad, (0, 0), (0, 0)),
        dimension_numbers=("NDHWC", "DHWIO", "NDHWC"),
        preferred_element_type=jnp.float32,
    )
    return out[0]


def inside(axis, size, width):
    total = size * lax.axis_size(axis)
    start = lax.axis_index(axis) * size - width
    index = start + jnp.arange(size + 2 * width)
    return (index >= 0) & (index < total)


def local(latents, first_gain, first_weight, first_bias, second_gain, second_weight, second_bias):
    frames, rows, cols, chans = latents.shape
    values = latents.astype(jnp.float32)
    first_act = jax.nn.silu(rms_norm(values, first_gain)).astype(jnp.bfloat16)
    stack = jnp.concatenate([shifted(first_act, "tm", 1), first_act], axis=0)
    wide = with_halo(stack, (("col", 2),), 2)
    middle = conv_valid(wide, first_weight)
    first_ext = with_halo(wide, (("row", 1),), 2)
    edge = 2 * 2
    top = conv_valid(first_ext[:, :edge], first_weight)
    bottom = conv_valid(first_ext[:, first_ext.shape[1] - edge :], first_weight)
    hidden = jnp.concatenate(
        [(piece + first_bias).astype(jnp.bfloat16) for piece in (top, middle, bottom)], axis=1
    )
    second_act = jax.nn.silu(rms_norm(hidden.astype(jnp.float32), second_gain))
    keep = inside("row", rows, 1)[:, None] & inside("col", cols, 1)[None, :]
    second_act = jnp.where(keep[None, :, :, None], second_act, 0.0).astype(jnp.bfloat16)
    ahead = conv_valid(second_act, second_weight[0:2], (0, 1)).astype(jnp.bfloat16)
    behind = shifted(ahead, "tm", 1)
    own = conv_valid(second_act, second_weight[1:3], (1, 0))
    decoded = values + own + behind.astype(jnp.float32) + second_bias
    return decoded.astype(jnp.bfloat16)


def solution(mesh):
    in_specs = (P("tm", "row", "col", None), P(), P(), P(), P(), P(), P())
    out_specs = P("tm", "row", "col", None)
    return jax.shard_map(local, mesh=mesh, in_specs=in_specs, out_specs=out_specs, check_vma=False)
```

```python
import jax
import jax.numpy as jnp
from jax import lax
from jax.sharding import PartitionSpec as P


def with_halo(cells, sides, width):
    for axis, dim in sides:
        count = lax.axis_size(axis)
        ends = count - 1
        head = lax.slice_in_dim(cells, 0, width, axis=dim)
        tail = lax.slice_in_dim(cells, cells.shape[dim] - width, cells.shape[dim], axis=dim)
        cells = jnp.concatenate(
            [
                lax.ppermute(tail, axis, [(i, i + 1) for i in range(ends)]),
                cells,
                lax.ppermute(head, axis, [(i + 1, i) for i in range(ends)]),
            ],
            axis=dim,
        )
    return cells


def shifted(value, axis, steps):
    count = lax.axis_size(axis)
    initial, last = (max(0, -steps), min(count, count - steps))
    return lax.ppermute(value, axis, [(source, source + steps) for source in range(initial, last)])


def rms_norm(values, gain):
    return values * lax.rsqrt(jnp.mean(values * values, axis=-1, keepdims=True) + 1e-06) * gain


def conv_valid(stack, kernel, frame_pad=(0, 0)):
    out = lax.conv_general_dilated(
        stack[None],
        kernel,
        window_strides=(1, 1, 1),
        padding=(frame_pad, (0, 0), (0, 0)),
        dimension_numbers=("NDHWC", "DHWIO", "NDHWC"),
        preferred_element_type=jnp.float32,
    )
    return out[0]


def inside(axis, size, width):
    total = size * lax.axis_size(axis)
    start = lax.axis_index(axis) * size - width
    index = start + jnp.arange(size + 2 * width)
    return (index >= 0) & (index < total)


def local(latents, first_gain, first_weight, first_bias, second_gain, second_weight, second_bias):
    frames, rows, cols, chans = latents.shape
    values = latents.astype(jnp.float32)
    first_act = jax.nn.silu(rms_norm(values, first_gain)).astype(jnp.bfloat16)
    stack = jnp.concatenate([shifted(first_act, "tm", 1), first_act], axis=0)
    wide = with_halo(stack, (("col", 2),), 2)
    middle = conv_valid(wide, first_weight)
    first_ext = with_halo(wide, (("row", 1),), 2)
    edge = 2 * 2
    top = conv_valid(first_ext[:, :edge], first_weight)
    bottom = conv_valid(first_ext[:, first_ext.shape[1] - edge :], first_weight)
    keep = inside("row", rows, 1)[:, None] & inside("col", cols, 1)[None, :]
    limits = (0, top.shape[1], top.shape[1] + middle.shape[1], keep.shape[0])
    pieces = []
    for index, piece in enumerate((top, middle, bottom)):
        hidden = (piece + first_bias).astype(jnp.bfloat16).astype(jnp.float32)
        act = jax.nn.silu(rms_norm(hidden, second_gain))
        mask = keep[limits[index] : limits[index + 1]]
        pieces.append(jnp.where(mask[None, :, :, None], act, 0.0).astype(jnp.bfloat16))
    second_act = jnp.concatenate(pieces, axis=1)
    ahead = conv_valid(second_act, second_weight[0:2], (0, 1)).astype(jnp.bfloat16)
    behind = shifted(ahead, "tm", 1)
    own = conv_valid(second_act, second_weight[1:3], (1, 0))
    decoded = values + own + behind.astype(jnp.float32) + second_bias
    return decoded.astype(jnp.bfloat16)


def solution(mesh):
    in_specs = (P("tm", "row", "col", None), P(), P(), P(), P(), P(), P())
    out_specs = P("tm", "row", "col", None)
    return jax.shard_map(local, mesh=mesh, in_specs=in_specs, out_specs=out_specs, check_vma=False)
```

```python
import jax
import jax.numpy as jnp
from jax import lax
from jax.sharding import PartitionSpec as P


def with_halo(cells, sides, width):
    for axis, dim in sides:
        count = lax.axis_size(axis)
        ends = count - 1
        head = lax.slice_in_dim(cells, 0, width, axis=dim)
        tail = lax.slice_in_dim(cells, cells.shape[dim] - width, cells.shape[dim], axis=dim)
        cells = jnp.concatenate(
            [
                lax.ppermute(tail, axis, [(i, i + 1) for i in range(ends)]),
                cells,
                lax.ppermute(head, axis, [(i + 1, i) for i in range(ends)]),
            ],
            axis=dim,
        )
    return cells


def shifted(value, axis, steps):
    count = lax.axis_size(axis)
    initial, last = (max(0, -steps), min(count, count - steps))
    return lax.ppermute(value, axis, [(source, source + steps) for source in range(initial, last)])


def rms_norm(values, gain):
    return values * lax.rsqrt(jnp.mean(values * values, axis=-1, keepdims=True) + 1e-06) * gain


def conv_valid(stack, kernel, frame_pad=(0, 0)):
    out = lax.conv_general_dilated(
        stack[None],
        kernel,
        window_strides=(1, 1, 1),
        padding=(frame_pad, (0, 0), (0, 0)),
        dimension_numbers=("NDHWC", "DHWIO", "NDHWC"),
        preferred_element_type=jnp.float32,
    )
    return out[0]


def inside(axis, size, width):
    total = size * lax.axis_size(axis)
    start = lax.axis_index(axis) * size - width
    index = start + jnp.arange(size + 2 * width)
    return (index >= 0) & (index < total)


def local(latents, first_gain, first_weight, first_bias, second_gain, second_weight, second_bias):
    frames, rows, cols, chans = latents.shape
    values = latents.astype(jnp.float32)
    first_act = jax.nn.silu(rms_norm(values, first_gain)).astype(jnp.bfloat16)
    stack = jnp.concatenate([shifted(first_act, "tm", 1), first_act], axis=0)
    wide = with_halo(stack, (("col", 2),), 2)
    middle = conv_valid(wide, first_weight)
    first_ext = with_halo(wide, (("row", 1),), 2)
    edge = 2 * 2
    top = conv_valid(first_ext[:, :edge], first_weight)
    bottom = conv_valid(first_ext[:, first_ext.shape[1] - edge :], first_weight)
    keep = inside("row", rows, 1)[:, None] & inside("col", cols, 1)[None, :]
    limits = (0, top.shape[1], top.shape[1] + middle.shape[1], keep.shape[0])
    pieces = []
    for index, piece in enumerate((top, middle, bottom)):
        hidden = (piece + first_bias).astype(jnp.bfloat16).astype(jnp.float32)
        act = jax.nn.silu(rms_norm(hidden, second_gain))
        mask = keep[limits[index] : limits[index + 1]]
        pieces.append(jnp.where(mask[None, :, :, None], act, 0.0).astype(jnp.bfloat16))
    second_act = jnp.concatenate(pieces, axis=1)
    top_act, middle_act, bottom_act = pieces
    reach = middle_act.shape[1]
    parts = (
        jnp.concatenate([top_act, middle_act[:, :2]], axis=1),
        middle_act,
        jnp.concatenate([middle_act[:, reach - 2 :], bottom_act], axis=1),
    )
    ahead = jnp.concatenate(
        [conv_valid(part, second_weight[0:2], (0, 1)).astype(jnp.bfloat16) for part in parts], axis=1
    )
    behind = shifted(ahead, "tm", 1)
    own = conv_valid(second_act, second_weight[1:3], (1, 0))
    decoded = values + own + behind.astype(jnp.float32) + second_bias
    return decoded.astype(jnp.bfloat16)


def solution(mesh):
    in_specs = (P("tm", "row", "col", None), P(), P(), P(), P(), P(), P())
    out_specs = P("tm", "row", "col", None)
    return jax.shard_map(local, mesh=mesh, in_specs=in_specs, out_specs=out_specs, check_vma=False)
```

```python
import jax
import jax.numpy as jnp
from jax import lax
from jax.sharding import PartitionSpec as P


def with_halo(cells, sides, width):
    for axis, dim in sides:
        count = lax.axis_size(axis)
        ends = count - 1
        head = lax.slice_in_dim(cells, 0, width, axis=dim)
        tail = lax.slice_in_dim(cells, cells.shape[dim] - width, cells.shape[dim], axis=dim)
        cells = jnp.concatenate(
            [
                lax.ppermute(tail, axis, [(i, i + 1) for i in range(ends)]),
                cells,
                lax.ppermute(head, axis, [(i + 1, i) for i in range(ends)]),
            ],
            axis=dim,
        )
    return cells


def shifted(value, axis, steps):
    count = lax.axis_size(axis)
    initial, last = (max(0, -steps), min(count, count - steps))
    return lax.ppermute(value, axis, [(source, source + steps) for source in range(initial, last)])


def rms_norm(values, gain):
    return values * lax.rsqrt(jnp.mean(values * values, axis=-1, keepdims=True) + 1e-06) * gain


def conv_valid(stack, kernel, frame_pad=(0, 0)):
    out = lax.conv_general_dilated(
        stack[None],
        kernel,
        window_strides=(1, 1, 1),
        padding=(frame_pad, (0, 0), (0, 0)),
        dimension_numbers=("NDHWC", "DHWIO", "NDHWC"),
        preferred_element_type=jnp.float32,
    )
    return out[0]


def inside(axis, size, width):
    total = size * lax.axis_size(axis)
    start = lax.axis_index(axis) * size - width
    index = start + jnp.arange(size + 2 * width)
    return (index >= 0) & (index < total)


def local(latents, first_gain, first_weight, first_bias, second_gain, second_weight, second_bias):
    frames, rows, cols, chans = latents.shape
    values = latents.astype(jnp.float32)
    first_act = jax.nn.silu(rms_norm(values, first_gain)).astype(jnp.bfloat16)
    stack = jnp.concatenate([shifted(first_act, "tm", 1), first_act], axis=0)
    wide = with_halo(stack, (("col", 2),), 2)
    middle = conv_valid(wide, first_weight)
    first_ext = with_halo(wide, (("row", 1),), 2)
    edge = 2 * 2
    ends = jnp.concatenate([first_ext[:, :edge], first_ext[:, first_ext.shape[1] - edge :]], axis=1)
    joined = conv_valid(ends, first_weight)
    keep = inside("row", rows, 1)[:, None] & inside("col", cols, 1)[None, :]
    span = middle.shape[1]

    def activated(piece, mask):
        hidden = (piece + first_bias).astype(jnp.bfloat16).astype(jnp.float32)
        act = jax.nn.silu(rms_norm(hidden, second_gain))
        return jnp.where(mask[None, :, :, None], act, 0.0).astype(jnp.bfloat16)

    middle_act = activated(middle, keep[2 : 2 + span])
    edge_keep = jnp.concatenate([keep[:2], keep[:2], keep[2 + span :]], axis=0)
    edge_act = activated(joined, edge_keep)
    top_act, bottom_act = edge_act[:, :2], edge_act[:, 4:]
    pieces = (top_act, middle_act, bottom_act)
    second_act = jnp.concatenate(pieces, axis=1)
    ahead = conv_valid(second_act, second_weight[0:2], (0, 1)).astype(jnp.bfloat16)
    behind = shifted(ahead, "tm", 1)
    own = conv_valid(second_act, second_weight[1:3], (1, 0))
    decoded = values + own + behind.astype(jnp.float32) + second_bias
    return decoded.astype(jnp.bfloat16)


def solution(mesh):
    in_specs = (P("tm", "row", "col", None), P(), P(), P(), P(), P(), P())
    out_specs = P("tm", "row", "col", None)
    return jax.shard_map(local, mesh=mesh, in_specs=in_specs, out_specs=out_specs, check_vma=False)
```
